512 devices in a mesh: worker: 16 (over x, z_lo, core), fsdp: 32 (over z_hi, y).
Axes of the slice: x: 4, y: 8, z: 8 (z_hi: 4, z_lo: 2; z = z_hi * 2 + z_lo), core: 2. Of those that a mesh axis runs over, the one named last changes fastest.
Arguments:
- hidden: bfloat16 [9472, 65536], P('fsdp', 'worker'), may hold values from -6 to 6
- cotangent: bfloat16 [65536, 1792], P(('worker', 'fsdp')), may hold values from -6 to 6
- first_moment: bfloat16 [16, 9472, 1792], P('worker', 'fsdp'), may hold values from -0.0625 to 0.0625
- second_moment: bfloat16 [16, 9472, 1792], P('worker', 'fsdp'), may hold values from 1.21593475e-05 to 0.00024414062
- outer_momentum: bfloat16 [9472, 1792], P('fsdp', 'worker'), may hold values from -4 to 4
Outputs:
- new_momentum: float32 [9472, 1792], P('fsdp', 'worker')
The draws below stay inside these ranges and needn't reach their ends.
All inputs are finite; a program needn't handle non-finite values.
Results may differ from the reference program's by a relative error of at most 0.0003.
Values may be sent and summed in bfloat16 or wider, within the bound.
No kernel may reach another device: no remote copies, remote signals or barrier semaphores. Data moves between devices by JAX's collectives and lax.ppermute only.
A program may use at most 64 MiB of HBM per device.

```python
import math
import jax
import jax.numpy as jnp
from jax import lax

D = 1792
FF = 9472
WORKERS = 16
GROUP_TOK = 4096
TOKENS = 65536


def levels(rng, shape, shards, low, largest):
    level, own = 1.0, jax.random.fold_in(rng, 6)
    for axis_at, shards_of in shards:
        heights = jnp.exp(jax.random.uniform(jax.random.fold_in(own, axis_at), (shards_of,), jnp.float32, low / len(shards), largest / len(shards)))
        level = level * jnp.repeat(heights, shape[axis_at] // shards_of).reshape([-1 if axis == axis_at else 1 for axis in range(len(shape))])
    return level


def bell_draw(stream_key, extent, spread, bound, pieces=(), held_as=jnp.bfloat16):
    gain = levels(stream_key, extent, pieces, -0.22, 0.18) if pieces else 1.0
    entries = jax.random.normal(stream_key, extent, jnp.float32) * spread * gain
    return jnp.minimum(jnp.maximum(entries, -bound), bound).astype(held_as)


def setup_inputs(seed: int = 0) -> dict:
    key_of = jax.random.split(jax.random.key(seed), 6)
    hidden = bell_draw(key_of[0], (FF, TOKENS), 1.0, 6.0, ((0, 32), (1, 16)))
    cotangent = bell_draw(key_of[1], (TOKENS, D), 1.0, 6.0, ((0, 512),))
    first_moment = bell_draw(key_of[2], (WORKERS, FF, D), (0.3 * GROUP_TOK ** -0.5), 0.0625, ((0, 16), (1, 32)))
    second_moment = jnp.clip(jnp.exp(math.log(0.00024414062) - 2.9996462 * jax.random.uniform(key_of[3], (WORKERS, FF, D), jnp.float32) ** levels(key_of[3], (WORKERS, FF, D), ((0, 16), (1, 32)), -0.2, 0.2)), 1.2159347534179688e-05, 0.00024414062).astype(jnp.bfloat16)
    outer_momentum = bell_draw(key_of[4], (FF, D), 0.5, 4.0, ((0, 32), (1, 16)))
    return {"hidden": hidden, "cotangent": cotangent, "first_moment": first_moment, "second_moment": second_moment, "outer_momentum": outer_momentum}


def worker_term(hidden, cotangent, first_moment, second_moment, worker_index):
    offset = worker_index * GROUP_TOK
    hidden_rows = lax.dynamic_slice_in_dim(hidden, offset, GROUP_TOK, 1)
    cotangent_rows = lax.dynamic_slice_in_dim(cotangent, offset, GROUP_TOK, 0)
    gradient = jnp.dot(hidden_rows, cotangent_rows, preferred_element_type=jnp.float32) / GROUP_TOK
    first_new = 0.9 * first_moment[worker_index].astype(jnp.float32) + 0.1 * gradient
    second_new = 0.95 * second_moment[worker_index].astype(jnp.float32) + 0.05 * gradient * gradient
    return first_new / (jnp.sqrt(second_new) + 1e-08)

def reference(hidden, cotangent, first_moment, second_moment, outer_momentum):

    def accumulate(running, worker_index):
        return (running + worker_term(hidden, cotangent, first_moment, second_moment, worker_index), None)
    running, _ = lax.scan(accumulate, jnp.zeros((FF, D), jnp.float32), jnp.arange(WORKERS, dtype=jnp.int32))
    average = running / WORKERS
    return 0.9 * outer_momentum.astype(jnp.float32) + average
```

```python
import jax
import jax.numpy as jnp
from jax import lax
from jax.sharding import Mesh
from jax.sharding import PartitionSpec as P

W = ("wx", "wz", "wc")
F = ("fz", "fy")


def shards(hidden, cotangent, first_moment, second_moment, outer_momentum):
    gathered = lax.all_gather(cotangent, "fy", axis=0, tiled=True)
    gathered = lax.all_gather(gathered, "fz", axis=0, tiled=True)
    gradient = jnp.dot(hidden, gathered, preferred_element_type=jnp.float32) / gathered.shape[0]
    first_new = 0.9 * first_moment[0].astype(jnp.float32) + 0.1 * gradient
    second_new = 0.95 * second_moment[0].astype(jnp.float32) + 0.05 * gradient * gradient
    pseudo = first_new / (jnp.sqrt(second_new) + 1e-08)
    summed = lax.psum_scatter(pseudo, "wx", scatter_dimension=1, tiled=True)
    summed = lax.psum_scatter(summed, "wz", scatter_dimension=1, tiled=True)
    summed = lax.psum_scatter(summed, "wc", scatter_dimension=1, tiled=True)
    average = summed / 16
    return 0.9 * outer_momentum.astype(jnp.float32) + average


def solution(mesh):
    sizes = {"worker": (4, 2, 2), "fsdp": (4, 8)}
    fine = Mesh(mesh.devices.reshape(sizes["worker"] + sizes["fsdp"]), W + F)
    in_specs = (
        P(F, W),
        P(W + F, None),
        P(W, F, None),
        P(W, F, None),
        P(F, W),
    )
    out_specs = P(F, W)
    return jax.shard_map(shards, mesh=fine, in_specs=in_specs, out_specs=out_specs, check_vma=False)
```

```python
import jax
import jax.numpy as jnp
from jax import lax
from jax.sharding import PartitionSpec as P


def shards(hidden, cotangent, first_moment, second_moment, outer_momentum):
    gathered = lax.all_gather(cotangent, "fsdp", axis=0, tiled=True)
    gradient = jnp.dot(hidden, gathered, preferred_element_type=jnp.float32) / gathered.shape[0]
    first_new = 0.9 * first_moment[0].astype(jnp.float32) + 0.1 * gradient
    second_new = 0.95 * second_moment[0].astype(jnp.float32) + 0.05 * gradient * gradient
    pseudo = first_new / (jnp.sqrt(second_new) + 1e-08)
    workers = lax.axis_size("worker")
    rows, cols = pseudo.shape
    blocks = pseudo.reshape(rows, workers, cols // workers)
    received = lax.all_to_all(blocks, "worker", 1, 1, tiled=True)
    average = received.sum(axis=1) / workers
    return 0.9 * outer_momentum.astype(jnp.float32) + average


def solution(mesh):
    in_specs = (
        P("fsdp", "worker"),
        P(("worker", "fsdp"), None),
        P("worker", "fsdp", None),
        P("worker", "fsdp", None),
        P("fsdp", "worker"),
    )
    out_specs = P("fsdp", "worker")
    return jax.shard_map(shards, mesh=mesh, in_specs=in_specs, out_specs=out_specs, check_vma=False)
```

```python
import jax
import jax.numpy as jnp
from jax import lax
from jax.sharding import PartitionSpec as P

CHUNKS = 2


def shards(hidden, cotangent, first_moment, second_moment, outer_momentum):
    workers = lax.axis_size("worker")
    rows = hidden.shape[0]
    tokens_here, cols = cotangent.shape
    width = cols // workers // CHUNKS
    cot = cotangent.reshape(tokens_here, workers, CHUNKS, width)
    m1 = first_moment[0].reshape(rows, workers, CHUNKS, width)
    m2 = second_moment[0].reshape(rows, workers, CHUNKS, width)
    parts = []
    for j in range(CHUNKS):
        if parts:
            hidden, m1, m2, _ = lax.optimization_barrier((hidden, m1, m2, parts[-1]))
        piece = cot[:, :, j, :].reshape(tokens_here, workers * width)
        gathered = lax.all_gather(piece, "fsdp", axis=0, tiled=True)
        gradient = jnp.dot(hidden, gathered, preferred_element_type=jnp.float32) / gathered.shape[0]
        gradient = gradient.reshape(rows, workers, width)
        first_new = 0.9 * m1[:, :, j, :].astype(jnp.float32) + 0.1 * gradient
        second_new = 0.95 * m2[:, :, j, :].astype(jnp.float32) + 0.05 * gradient * gradient
        pseudo = first_new / (jnp.sqrt(second_new) + 1e-08)
        received = lax.all_to_all(pseudo, "worker", 1, 1, tiled=True)
        parts.append(received.sum(axis=1) / workers)
    average = jnp.stack(parts, axis=1).reshape(rows, CHUNKS * width)
    return 0.9 * outer_momentum.astype(jnp.float32) + average


def solution(mesh):
    in_specs = (
        P("fsdp", "worker"),
        P(("worker", "fsdp"), None),
        P("worker", "fsdp", None),
        P("worker", "fsdp", None),
        P("fsdp", "worker"),
    )
    out_specs = P("fsdp", "worker")
    return jax.shard_map(shards, mesh=mesh, in_specs=in_specs, out_specs=out_specs, check_vma=False)
```

```python
import jax
import jax.numpy as jnp
from jax import lax
from jax.sharding import PartitionSpec as P


def shards(hidden, cotangent, first_moment, second_moment, outer_momentum):
    flat = lax.all_gather(cotangent.reshape(-1), "fsdp", axis=0, tiled=True)
    gathered = flat.reshape(-1, cotangent.shape[1])
    gradient = jnp.dot(hidden, gathered, preferred_element_type=jnp.float32) / gathered.shape[0]
    first_new = 0.9 * first_moment[0].astype(jnp.float32) + 0.1 * gradient
    second_new = 0.95 * second_moment[0].astype(jnp.float32) + 0.05 * gradient * gradient
    pseudo = first_new / (jnp.sqrt(second_new) + 1e-08)
    workers = lax.axis_size("worker")
    rows, cols = pseudo.shape
    blocks = pseudo.reshape(rows, workers, cols // workers)
    received = lax.all_to_all(blocks, "worker", 1, 1, tiled=True)
    average = received.sum(axis=1) / workers
    return 0.9 * outer_momentum.astype(jnp.float32) + average


def solution(mesh):
    in_specs = (
        P("fsdp", "worker"),
        P(("worker", "fsdp"), None),
        P("worker", "fsdp", None),
        P("worker", "fsdp", None),
        P("fsdp", "worker"),
    )
    out_specs = P("fsdp", "worker")
    return jax.shard_map(shards, mesh=mesh, in_specs=in_specs, out_specs=out_specs, check_vma=False)
```

```python
import jax
import jax.numpy as jnp
from jax import lax
from jax.sharding import PartitionSpec as P


def shards(hidden, cotangent, first_moment, second_moment, outer_momentum):
    workers = lax.axis_size("worker")
    rows = hidden.shape[0]
    cols = cotangent.shape[1]
    gathered = lax.all_gather(cotangent, "fsdp", axis=0, tiled=True)
    tokens = gathered.shape[0]
    cut = (rows // 2 + 7) // 8 * 8
    m1, m2 = first_moment[0], second_moment[0]
    parts = []
    for lo, hi in ((0, cut), (cut, rows)):
        if parts:
            hidden, m1, m2, _ = lax.optimization_barrier((hidden, m1, m2, parts[-1]))
        gradient = jnp.dot(hidden[lo:hi], gathered, preferred_element_type=jnp.float32) / tokens
        first_new = 0.9 * m1[lo:hi].astype(jnp.float32) + 0.1 * gradient
        second_new = 0.95 * m2[lo:hi].astype(jnp.float32) + 0.05 * gradient * gradient
        pseudo = first_new / (jnp.sqrt(second_new) + 1e-08)
        blocks = pseudo.reshape(hi - lo, workers, cols // workers)
        received = lax.all_to_all(blocks, "worker", 1, 1, tiled=True)
        parts.append(received.sum(axis=1) / workers)
    average = jnp.concatenate(parts, axis=0)
    return 0.9 * outer_momentum.astype(jnp.float32) + average


def solution(mesh):
    in_specs = (
        P("fsdp", "worker"),
        P(("worker", "fsdp"), None),
        P("worker", "fsdp", None),
        P("worker", "fsdp", None),
        P("fsdp", "worker"),
    )
    out_specs = P("fsdp", "worker")
    return jax.shard_map(shards, mesh=mesh, in_specs=in_specs, out_specs=out_specs, check_vma=False)
```

```python
import jax
import jax.numpy as jnp
from jax import lax
from jax.sharding import PartitionSpec as P


def shards(hidden, cotangent, first_moment, second_moment, outer_momentum):
    gathered = lax.all_gather(cotangent, "fsdp", axis=0, tiled=True)
    gradient = jnp.dot(hidden, gathered, preferred_element_type=jnp.float32) / gathered.shape[0]
    first_new = 0.9 * first_moment[0].astype(jnp.float32) + 0.1 * gradient
    second_new = 0.95 * second_moment[0].astype(jnp.float32) + 0.05 * gradient * gradient
    pseudo = first_new / (jnp.sqrt(second_new) + 1e-08)
    workers = lax.axis_size("worker")
    rows, cols = pseudo.shape
    cut = rows // 4 // 8 * 8
    offloaded = lax.psum_scatter(pseudo[:cut], "worker", scatter_dimension=1, tiled=True)
    blocks = pseudo[cut:].reshape(rows - cut, workers, cols // workers)
    received = lax.all_to_all(blocks, "worker", 1, 1, tiled=True)
    average = jnp.concatenate([offloaded, received.sum(axis=1)], axis=0) / workers
    return 0.9 * outer_momentum.astype(jnp.float32) + average


def solution(mesh):
    in_specs = (
        P("fsdp", "worker"),
        P(("worker", "fsdp"), None),
        P("worker", "fsdp", None),
        P("worker", "fsdp", None),
        P("fsdp", "worker"),
    )
    out_specs = P("fsdp", "worker")
    return jax.shard_map(shards, mesh=mesh, in_specs=in_specs, out_specs=out_specs, check_vma=False)
```

```python
import jax
import jax.numpy as jnp
from jax import lax
from jax.sharding import Mesh
from jax.sharding import PartitionSpec as P

W = ("wx", "wz", "wc")
F = ("fz", "fy")
SPLIT = {"worker": (4, 2, 2), "fsdp": (4, 8)}


def shards(hidden, cotangent, first_moment, second_moment, outer_momentum):
    gathered = lax.all_gather(cotangent, F, axis=0, tiled=True)
    gradient = jnp.dot(hidden, gathered, preferred_element_type=jnp.float32) / gathered.shape[0]
    first_new = 0.9 * first_moment[0].astype(jnp.float32) + 0.1 * gradient
    second_new = 0.95 * second_moment[0].astype(jnp.float32) + 0.05 * gradient * gradient
    pseudo = first_new / (jnp.sqrt(second_new) + 1e-08)
    rows, cols = pseudo.shape
    nx, nz, nc = SPLIT["worker"]
    blocks = pseudo.reshape(rows, nx, nz, nc, cols // (nx * nz * nc))
    blocks = lax.all_to_all(blocks, "wc", 3, 3, tiled=True).sum(axis=3)
    blocks = lax.all_to_all(blocks, "wz", 2, 2, tiled=True).sum(axis=2)
    blocks = lax.all_to_all(blocks, "wx", 1, 1, tiled=True).sum(axis=1)
    average = blocks / (nx * nz * nc)
    return 0.9 * outer_momentum.astype(jnp.float32) + average


def solution(mesh):
    fine = Mesh(mesh.devices.reshape(SPLIT["worker"] + SPLIT["fsdp"]), W + F)
    in_specs = (
        P(F, W),
        P(W + F, None),
        P(W, F, None),
        P(W, F, None),
        P(F, W),
    )
    out_specs = P(F, W)
    return jax.shard_map(shards, mesh=fine, in_specs=in_specs, out_specs=out_specs, check_vma=False)
```

```python
import jax
import jax.numpy as jnp
from jax import lax
from jax.sharding import Mesh
from jax.sharding import PartitionSpec as P

W = ("wx", "wz", "wc")
F = ("fz", "fy")
SPLIT = {"worker": (4, 2, 2), "fsdp": (4, 8)}


def shards(hidden, cotangent, first_moment, second_moment, outer_momentum):
    gathered = lax.all_gather(cotangent, ("fy", "fz"), axis=0, tiled=True)
    nz, ny = SPLIT["fsdp"]
    rows, tokens = hidden.shape
    reordered = hidden.reshape(rows, nz, ny, tokens // (nz * ny)).transpose(0, 2, 1, 3).reshape(rows, tokens)
    gradient = jnp.dot(reordered, gathered, preferred_element_type=jnp.float32) / gathered.shape[0]
    first_new = 0.9 * first_moment[0].astype(jnp.float32) + 0.1 * gradient
    second_new = 0.95 * second_moment[0].astype(jnp.float32) + 0.05 * gradient * gradient
    pseudo = first_new / (jnp.sqrt(second_new) + 1e-08)
    workers = lax.axis_size(W)
    cols = pseudo.shape[1]
    blocks = pseudo.reshape(rows, workers, cols // workers)
    received = lax.all_to_all(blocks, W, 1, 1, tiled=True)
    average = received.sum(axis=1) / workers
    return 0.9 * outer_momentum.astype(jnp.float32) + average


def solution(mesh):
    fine = Mesh(mesh.devices.reshape(SPLIT["worker"] + SPLIT["fsdp"]), W + F)
    in_specs = (
        P(F, W),
        P(W + F, None),
        P(W, F, None),
        P(W, F, None),
        P(F, W),
    )
    out_specs = P(F, W)
    return jax.shard_map(shards, mesh=fine, in_specs=in_specs, out_specs=out_specs, check_vma=False)
```

```python
import jax
import jax.numpy as jnp
from jax import lax
from jax.sharding import Mesh
from jax.sharding import PartitionSpec as P

W = ("wx", "wz", "wc")
F = ("fz", "fy")
SPLIT = {"worker": (4, 2, 2), "fsdp": (4, 8)}


def shards(hidden, cotangent, first_moment, second_moment, outer_momentum):
    gathered = lax.all_gather(cotangent, ("fy", "fz"), axis=0, tiled=True)
    nz, ny = SPLIT["fsdp"]
    rows, tokens = hidden.shape
    reordered = hidden.reshape(rows, nz, ny, tokens // (nz * ny)).transpose(0, 2, 1, 3).reshape(rows, tokens)
    gradient = jnp.dot(reordered, gathered, preferred_element_type=jnp.float32) / gathered.shape[0]
    gradient = lax.optimization_barrier(gradient)
    workers = lax.axis_size(W)
    cols = gradient.shape[1]

    def blocked(x):
        return x.reshape(rows, workers, cols // workers).transpose(1, 0, 2)

    first_new = 0.9 * blocked(first_moment[0]).astype(jnp.float32) + 0.1 * blocked(gradient)
    second_new = 0.95 * blocked(second_moment[0]).astype(jnp.float32) + 0.05 * blocked(gradient) * blocked(gradient)
    pseudo = first_new / (jnp.sqrt(second_new) + 1e-08)
    received = lax.all_to_all(pseudo, W, 0, 0, tiled=True)
    average = received.sum(axis=0) / workers
    return 0.9 * outer_momentum.astype(jnp.float32) + average


def solution(mesh):
    fine = Mesh(mesh.devices.reshape(SPLIT["worker"] + SPLIT["fsdp"]), W + F)
    in_specs = (
        P(F, W),
        P(W + F, None),
        P(W, F, None),
        P(W, F, None),
        P(F, W),
    )
    out_specs = P(F, W)
    return jax.shard_map(shards, mesh=fine, in_specs=in_specs, out_specs=out_specs, check_vma=False)
```

```python
import jax
import jax.numpy as jnp
from jax import lax
from jax.sharding import Mesh
from jax.sharding import PartitionSpec as P

W = ("wx", "wz", "wc")
F = ("fz", "fy")
SPLIT = {"worker": (4, 2, 2), "fsdp": (4, 8)}


def shards(hidden, cotangent, first_moment, second_moment, outer_momentum):
    gathered = lax.all_gather(cotangent, ("fy", "fz"), axis=0, tiled=True)
    nz, ny = SPLIT["fsdp"]
    rows, tokens = hidden.shape
    reordered = hidden.reshape(rows, nz, ny, tokens // (nz * ny)).transpose(0, 2, 1, 3).reshape(rows, tokens)
    gradient = jnp.dot(reordered, gathered, preferred_element_type=jnp.float32) / gathered.shape[0]
    first_new = 0.9 * first_moment[0].astype(jnp.float32) + 0.1 * gradient
    second_new = 0.95 * second_moment[0].astype(jnp.float32) + 0.05 * gradient * gradient
    pseudo = first_new / (jnp.sqrt(second_new) + 1e-08)
    workers = lax.axis_size(W)
    cols = pseudo.shape[1]
    nx, nz, nc = SPLIT["worker"]
    blocks = pseudo.reshape(rows, nx, nz, nc, cols // workers).transpose(0, 3, 2, 1, 4)
    blocks = blocks.reshape(rows, workers, cols // workers)
    received = lax.all_to_all(blocks, W[::-1], 1, 1, tiled=True)
    average = received.sum(axis=1) / workers
    return 0.9 * outer_momentum.astype(jnp.float32) + average


def solution(mesh):
    fine = Mesh(mesh.devices.reshape(SPLIT["worker"] + SPLIT["fsdp"]), W + F)
    in_specs = (
        P(F, W),
        P(W + F, None),
        P(W, F, None),
        P(W, F, None),
        P(F, W),
    )
    out_specs = P(F, W)
    return jax.shard_map(shards, mesh=fine, in_specs=in_specs, out_specs=out_specs, check_vma=False)
```
